256 devices in a mesh: dp: 64 (over z, y, core), fsdp: 4 (over x).
Axes of the slice: x: 4, y: 4, z: 8, core: 2. Of those that a mesh axis runs over, the one named last changes fastest.
Arguments:
- feats: bfloat16 [64, 4, 8, 128, 256], P('dp', 'fsdp'), may hold values from -6 to 6
- grad_out: bfloat16 [64, 4, 8, 128, 256], P('dp', 'fsdp'), may hold values from -6 to 6
- kernel: bfloat16 [27, 256, 256], P(None, 'fsdp'), may hold values from -0.25 to 0.25
- send_bricks: int32 [64, 4, 64, 2], P('dp', 'fsdp'), may hold values from -1 to 7, as said below
- kmap: int32 [64, 4, 27, 2, 3], P('dp', 'fsdp'), may hold values from 0 to 135, as said below
- pair_count: int32 [64, 4, 27], P('dp', 'fsdp'), may hold values from 1 to 3, as said below
Outputs:
- out_feats: bfloat16 [64, 4, 8, 128, 256], P('dp', 'fsdp')
- in_grad: bfloat16 [64, 4, 8, 128, 256], P('dp', 'fsdp')
- kernel_grad: float32 [27, 256, 256], P(None, 'fsdp')
The draws below stay inside these ranges and needn't reach their ends.
Inputs may be any that keep to these rules, and one draw needn't show every extreme that they name: `send_bricks`: entry (d, f, p, c) names the brick of device (d, f) sent to device (p, f) in slot c, or -1 for an empty slot. A device sends nothing to itself, fills exactly 48 slots, and fills both slots of at least one peer. kmap[d, f, t, 0, s] is an input brick of pool[d, f]: below 8 an own brick, else received slot p * 2 + c after the 8 own ones, and then always a slot that its sender filled. kmap[d, f, t, 1, s] is an output brick, below 8. Slots that are not live hold such ids too. `pair_count`: on some device every offset has 3 live slots.
All inputs are finite; a program needn't handle non-finite values.
Results may differ from the reference program's by a relative error of at most 0.0046.
Values may be sent and summed in bfloat16 or wider, within the bound.
No kernel may reach another device: no remote copies, remote signals or barrier semaphores. Data moves between devices by JAX's collectives and lax.ppermute only.
A program may use at most 192 MiB of HBM per device.

```python
import jax
import jax.numpy as jnp
from jax import lax

C = 256
TAPS = 27
BRICK = 128
CAP = 2
SLOTS = 3
BR = 8
PEERS = 64
COLUMNS = 4
GHOST = 48
POOL = 136
GRAD_DIV = 1024
N_DP = 64
N_FSDP = 4


def shared_tables(key):
    base = jax.random.fold_in(key, 101)
    keys = jax.random.split(base, 9)
    span = (PEERS - 1) * CAP
    slot_ids = jnp.arange(span, dtype=jnp.int32)
    noise = jax.random.randint(keys[0], (PEERS, COLUMNS, span), 0, 2 ** 20)
    forced = jax.random.randint(keys[1], (PEERS, COLUMNS, 1), 0, PEERS - 1)
    score = jnp.where(slot_ids // CAP == forced, slot_ids - span, noise * span + slot_ids)
    order = jnp.argsort(score, axis=-1)
    ranks = jnp.argsort(order, axis=-1)
    chosen = ranks < GHOST
    bricks = jax.random.randint(keys[2], (PEERS, COLUMNS, span), 0, BR)
    picked = jnp.where(chosen, bricks, -1).astype(jnp.int32)
    sender = jnp.arange(PEERS)[:, None, None]
    target = jnp.arange(PEERS)[None, :, None]
    within = jnp.arange(CAP)[None, None, :]
    offset = (target - sender - 1) % PEERS
    valid = offset < PEERS - 1
    safe_index = jnp.where(valid, offset * CAP + within, 0)
    picked_t = jnp.transpose(picked, (0, 2, 1))
    table = picked_t[sender, safe_index]
    table = jnp.where(valid[:, :, :, None], table, -1)
    send = jnp.transpose(table, (0, 3, 1, 2)).astype(jnp.int32)
    filled = jnp.transpose(send, (2, 1, 0, 3)) >= 0
    fill_flat = filled.reshape(PEERS, COLUMNS, PEERS * CAP)
    fill_total = jnp.sum(fill_flat.astype(jnp.int32), axis=-1)
    ghost_order = jnp.argsort(jnp.where(fill_flat, 0, 1) * (PEERS * CAP) + jnp.arange(PEERS * CAP), axis=-1)
    valid_total = BR + fill_total
    choose = jax.random.randint(keys[3], (PEERS, COLUMNS, TAPS, SLOTS), 0, 2 ** 20) % valid_total[:, :, None, None]
    ghost_pos = jnp.clip(choose - BR, 0, PEERS * CAP - 1).reshape(PEERS, COLUMNS, TAPS * SLOTS)
    ghost_ids = BR + jnp.take_along_axis(ghost_order, ghost_pos, axis=-1).reshape(PEERS, COLUMNS, TAPS, SLOTS)
    source_ids = jnp.where(choose < BR, choose, ghost_ids)
    target_ids = jax.random.randint(keys[4], (PEERS, COLUMNS, TAPS, SLOTS), 0, BR)
    kernel_map = jnp.stack([source_ids, target_ids], axis=3).astype(jnp.int32)
    first = jax.random.randint(keys[5], (PEERS, COLUMNS), 0, SLOTS)
    second = jax.random.randint(keys[6], (PEERS, COLUMNS), 0, SLOTS)
    levels = 1 + first * second // SLOTS
    heavy = jax.random.randint(keys[7], (), 0, PEERS * COLUMNS)
    device_ids = jnp.arange(PEERS * COLUMNS).reshape(PEERS, COLUMNS)
    minus = jax.random.randint(keys[8], (PEERS, COLUMNS, TAPS), 0, 2)
    counts = jnp.maximum(1, levels[:, :, None] - minus)
    counts = jnp.where(device_ids[:, :, None] == heavy, SLOTS, counts).astype(jnp.int32)
    return (send, kernel_map, counts)


def draw_send_bricks(key, part):
    return shared_tables(key)[0]


def draw_kmap(key, part):
    return shared_tables(key)[1]


def draw_pair_count(key, part):
    return shared_tables(key)[2]


def block_scale(key, dims, pieces, low, high):
    def one(dim, parts):
        heights = jax.random.uniform(jax.random.fold_in(jax.random.fold_in(key, 6), dim), (parts,), jnp.float32, low / len(pieces), high / len(pieces))
        return jnp.repeat(jnp.exp(heights), dims[dim] // parts).reshape((-1,) + (1,) * (len(dims) - dim - 1))

    gain = one(*pieces[0])
    for cut in pieces[1:]:
        gain = gain * one(*cut)
    return gain


def normal_values(stream_key, extent, width, most, cuts=(), kind=jnp.bfloat16):
    entries = jax.random.normal(stream_key, extent, jnp.float32) * width
    if len(cuts) > 0:
        entries = block_scale(stream_key, extent, cuts, -0.22, 0.18) * entries
    return jnp.clip(entries, min=-most, max=most).astype(kind)


def setup_inputs(seed: int = 0) -> dict:
    key_list = jax.random.split(jax.random.key(seed), 7)
    feats = normal_values(key_list[0], (PEERS, COLUMNS, BR, BRICK, C), 1.0, 6.0, ((0, 64), (1, 4)))
    grad_out = normal_values(key_list[1], (PEERS, COLUMNS, BR, BRICK, C), 1.0, 6.0, ((0, 64), (1, 4)))
    kernel = normal_values(key_list[2], (TAPS, C, C), (2 * C) ** -0.5, 0.25, ((1, 4),))
    send_bricks = draw_send_bricks(jax.random.fold_in(key_list[6], 71), 0)
    kmap = draw_kmap(jax.random.fold_in(key_list[6], 71), 0)
    pair_count = draw_pair_count(jax.random.fold_in(key_list[6], 71), 0)
    return {"feats": feats, "grad_out": grad_out, "kernel": kernel, "send_bricks": send_bricks, "kmap": kmap, "pair_count": pair_count}


def device_terms(own_rows, upstream_rows, weights, incoming, source_map, target_map, counts):
    pool = jnp.concatenate([own_rows, incoming.reshape(-1, BRICK, C)], axis=0)
    active = (jnp.arange(SLOTS)[None, :] < counts[:, None]).astype(jnp.float32)
    inputs = pool[source_map].astype(jnp.float32) * active[:, :, None, None]
    upstream = upstream_rows[target_map].astype(jnp.float32) * active[:, :, None, None]
    contrib = jnp.einsum('tsvc,tcd->tsvd', inputs, weights, precision=lax.Precision.HIGHEST)
    produced = jax.ops.segment_sum(contrib.reshape(TAPS * SLOTS, BRICK, C), target_map.reshape(-1), num_segments=BR)
    backward = jnp.einsum('tsvd,tcd->tsvc', upstream, weights, precision=lax.Precision.HIGHEST)
    pool_grad = jax.ops.segment_sum(backward.reshape(TAPS * SLOTS, BRICK, C), source_map.reshape(-1), num_segments=POOL)
    partial_value = jnp.einsum('tsvc,tsvd->tcd', inputs, upstream, precision=lax.Precision.HIGHEST)
    return produced, pool_grad, partial_value


def reference(feats, grad_out, kernel, send_bricks, kmap, pair_count):
    weights = kernel.astype(jnp.float32)
    peer_ids = jnp.arange(N_DP).astype(jnp.int32)
    produced_columns = []
    grad_columns = []
    kernel_sum = jnp.zeros((TAPS, C, C), jnp.float32)
    for column_index in range(N_FSDP):
        def advance(carry, receiver):
            input_sum, kernel_acc = carry
            senders = send_bricks[:, column_index, receiver, :]
            filled = (senders >= 0)
            incoming = feats[peer_ids[:, None], column_index, jnp.maximum(senders, 0)]
            incoming = incoming * filled[:, :, None, None].astype(jnp.bfloat16)
            produced, pool_grad, partial_value = device_terms(
                feats[receiver, column_index], grad_out[receiver, column_index], weights, incoming,
                kmap[receiver, column_index, :, 0, :], kmap[receiver, column_index, :, 1, :],
                pair_count[receiver, column_index])
            rounded = lax.optimization_barrier(pool_grad[BR:].astype(jnp.bfloat16))
            ghosts = rounded.astype(jnp.float32).reshape(N_DP, CAP, BRICK, C)
            input_sum = input_sum.at[receiver].add(pool_grad[:BR])
            owners = jnp.where(filled, senders, BR).astype(jnp.int32)
            input_sum = input_sum.at[peer_ids[:, None], owners].add(ghosts, mode="drop")
            return (input_sum, kernel_acc + partial_value), produced.astype(jnp.bfloat16)
        start = (jnp.zeros((N_DP, BR, BRICK, C), jnp.float32), jnp.zeros((TAPS, C, C), jnp.float32))
        (input_sum, kernel_acc), produced_all = lax.scan(advance, start, peer_ids)
        produced_columns.append(produced_all)
        grad_columns.append(input_sum.astype(jnp.bfloat16))
        kernel_sum = kernel_sum + kernel_acc
    out_feats = jnp.stack(produced_columns, axis=1)
    in_grad = jnp.stack(grad_columns, axis=1)
    kernel_grad = kernel_sum / jnp.float32(GRAD_DIV)
    return out_feats, in_grad, kernel_grad
```

```python
import jax
import jax.numpy as jnp
from jax import lax
from jax.sharding import PartitionSpec as P


def _onehot(index, size, dtype):
    return (index[..., None] == jnp.arange(size, dtype=index.dtype)).astype(dtype)


def on_device(feats, grad_out, kernel, send_bricks, kmap, pair_count):
    own_rows = feats[0, 0]
    upstream_rows = grad_out[0, 0]
    senders = send_bricks[0, 0]
    peer_total, slot_cap = senders.shape
    brick_total, brick_rows, channels = own_rows.shape
    ghost_total = peer_total * slot_cap
    own_flat = own_rows.reshape(brick_total, brick_rows * channels)
    up_flat = upstream_rows.reshape(brick_total, brick_rows * channels)

    send_pick = _onehot(senders.reshape(-1), brick_total, jnp.bfloat16)
    outgoing = jnp.dot(send_pick, own_flat, preferred_element_type=jnp.float32).astype(jnp.bfloat16)
    outgoing = outgoing.reshape(peer_total, slot_cap, brick_rows, channels)
    incoming = lax.all_to_all(outgoing, "dp", split_axis=0, concat_axis=0, tiled=True)

    weights = lax.all_gather(kernel, "fsdp", axis=1, tiled=True)
    source_map = kmap[0, 0, :, 0, :]
    target_map = kmap[0, 0, :, 1, :]
    counts = pair_count[0, 0]
    tap_total, slot_total = source_map.shape
    pair_total = tap_total * slot_total
    active = jnp.arange(slot_total)[None, :] < counts[:, None]
    src = source_map.reshape(-1)
    tgt = target_map.reshape(-1)
    live = active.reshape(-1)

    up_pick = _onehot(tgt, brick_total, jnp.bfloat16) * live[:, None].astype(jnp.bfloat16)
    upstream = jnp.dot(up_pick, up_flat, preferred_element_type=jnp.float32).astype(jnp.bfloat16)
    upstream = upstream.reshape(tap_total, slot_total, brick_rows, channels)
    backward = jnp.einsum("tsvd,tcd->tsvc", upstream, weights, preferred_element_type=jnp.float32)
    backward = backward.reshape(pair_total, brick_rows * channels)
    src_pick = _onehot(src, brick_total + ghost_total, jnp.float32).T
    ghost_grad = jnp.dot(
        src_pick[brick_total:], backward, precision=lax.Precision.HIGHEST,
        preferred_element_type=jnp.float32,
    ).astype(jnp.bfloat16)
    own_grad = jnp.dot(
        src_pick[:brick_total], backward, precision=lax.Precision.HIGHEST,
        preferred_element_type=jnp.float32,
    )
    returned = lax.all_to_all(
        ghost_grad.reshape(peer_total, slot_cap, brick_rows, channels),
        "dp", split_axis=0, concat_axis=0, tiled=True,
    )

    in_pick = _onehot(src, brick_total + ghost_total, jnp.bfloat16) * live[:, None].astype(jnp.bfloat16)
    inc_flat = incoming.reshape(ghost_total, brick_rows * channels)
    inputs = (
        jnp.dot(in_pick[:, :brick_total], own_flat, preferred_element_type=jnp.float32)
        + jnp.dot(in_pick[:, brick_total:], inc_flat, preferred_element_type=jnp.float32)
    ).astype(jnp.bfloat16)
    inputs = inputs.reshape(tap_total, slot_total, brick_rows, channels)
    contrib = jnp.einsum("tsvc,tcd->tsvd", inputs, weights, preferred_element_type=jnp.float32)
    out_pick = _onehot(tgt, brick_total, jnp.float32).T
    produced = jnp.dot(
        out_pick, contrib.reshape(pair_total, brick_rows * channels),
        precision=lax.Precision.HIGHEST, preferred_element_type=jnp.float32,
    )
    produced = produced.reshape(brick_total, brick_rows, channels).astype(jnp.bfloat16)

    partial_value = jnp.einsum(
        "tsvc,tsvd->tcd", inputs, upstream, preferred_element_type=jnp.float32
    )
    divisor = jnp.float32(4 * lax.axis_size("dp") * lax.axis_size("fsdp"))
    scattered = lax.psum_scatter(partial_value, "fsdp", scatter_dimension=1, tiled=True)
    kernel_grad = lax.psum(scattered, "dp") / divisor

    owner_pick = _onehot(senders.reshape(-1), brick_total, jnp.bfloat16).T
    back_sum = jnp.dot(
        owner_pick, returned.reshape(ghost_total, brick_rows * channels),
        preferred_element_type=jnp.float32,
    )
    in_grad = (own_grad + back_sum).reshape(brick_total, brick_rows, channels).astype(jnp.bfloat16)
    return (produced[None, None], in_grad[None, None], kernel_grad)


def solution(mesh):
    placed = (
        P("dp", "fsdp", None, None, None),
        P("dp", "fsdp", None, None, None),
        P(None, "fsdp", None),
        P("dp", "fsdp", None, None),
        P("dp", "fsdp", None, None, None),
        P("dp", "fsdp", None),
    )
    return jax.shard_map(
        on_device,
        mesh=mesh,
        in_specs=placed,
        out_specs=(
            P("dp", "fsdp", None, None, None),
            P("dp", "fsdp", None, None, None),
            P(None, "fsdp", None),
        ),
        check_vma=False,
    )
```

```python
import jax
import jax.numpy as jnp
from jax import lax
from jax.sharding import PartitionSpec as P


def _onehot(index, size, dtype):
    return (index[..., None] == jnp.arange(size, dtype=index.dtype)).astype(dtype)


def _halving_doubling_sum(value, axis):
    size = lax.axis_size(axis)
    steps = size.bit_length() - 1
    assert 1 << steps == size
    me = lax.axis_index(axis)
    shape = value.shape
    buf = value.reshape(-1)
    total = buf.shape[0]
    assert total % size == 0
    for k in range(steps):
        half = buf.shape[0] // 2
        bit = (me >> k) & 1
        keep = lax.dynamic_slice_in_dim(buf, bit * half, half)
        send = lax.dynamic_slice_in_dim(buf, (1 - bit) * half, half)
        pairs = [(i, i ^ (1 << k)) for i in range(size)]
        buf = keep + lax.ppermute(send, axis, pairs)
    for k in reversed(range(steps)):
        part = buf.shape[0]
        bit = (me >> k) & 1
        pairs = [(i, i ^ (1 << k)) for i in range(size)]
        other = lax.ppermute(buf, axis, pairs)
        whole = jnp.zeros((2 * part,), buf.dtype)
        whole = lax.dynamic_update_slice_in_dim(whole, buf, bit * part, 0)
        buf = lax.dynamic_update_slice_in_dim(whole, other, (1 - bit) * part, 0)
    return buf.reshape(shape)


def on_device(feats, grad_out, kernel, send_bricks, kmap, pair_count):
    own_rows = feats[0, 0]
    upstream_rows = grad_out[0, 0]
    senders = send_bricks[0, 0]
    peer_total, slot_cap = senders.shape
    brick_total, brick_rows, channels = own_rows.shape
    ghost_total = peer_total * slot_cap

    send_pick = _onehot(senders.reshape(-1), brick_total, jnp.bfloat16)
    outgoing = jnp.einsum("pb,bvd->pvd", send_pick, own_rows, preferred_element_type=jnp.float32)
    outgoing = outgoing.astype(jnp.bfloat16).reshape(peer_total, slot_cap, brick_rows, channels)
    incoming = lax.all_to_all(outgoing, "dp", split_axis=0, concat_axis=0, tiled=True)

    weights = lax.all_gather(kernel, "fsdp", axis=1, tiled=True)
    source_map = kmap[0, 0, :, 0, :]
    target_map = kmap[0, 0, :, 1, :]
    counts = pair_count[0, 0]
    tap_total, slot_total = source_map.shape
    pair_total = tap_total * slot_total
    active = jnp.arange(slot_total)[None, :] < counts[:, None]
    src = source_map.reshape(-1)
    tgt = target_map.reshape(-1)
    live = active.reshape(-1)

    up_pick = _onehot(tgt, brick_total, jnp.bfloat16) * live[:, None].astype(jnp.bfloat16)
    upstream = jnp.einsum("pb,bvd->pvd", up_pick, upstream_rows, preferred_element_type=jnp.float32)
    upstream = upstream.astype(jnp.bfloat16)
    upstream = upstream.reshape(tap_total, slot_total, brick_rows, channels)
    backward = jnp.einsum("tsvd,tcd->tsvc", upstream, weights, preferred_element_type=jnp.float32)
    backward = backward.reshape(pair_total, brick_rows, channels)
    src_pick = _onehot(src, brick_total + ghost_total, jnp.float32).T
    ghost_grad = jnp.einsum(
        "ip,pvd->ivd", src_pick[brick_total:], backward, precision=lax.Precision.HIGHEST,
        preferred_element_type=jnp.float32,
    ).astype(jnp.bfloat16)
    own_grad = jnp.einsum(
        "ip,pvd->ivd", src_pick[:brick_total], backward, precision=lax.Precision.HIGHEST,
        preferred_element_type=jnp.float32,
    )
    returned = lax.all_to_all(
        ghost_grad.reshape(peer_total, slot_cap, brick_rows, channels),
        "dp", split_axis=0, concat_axis=0, tiled=True,
    )

    in_pick = _onehot(src, brick_total + ghost_total, jnp.bfloat16) * live[:, None].astype(jnp.bfloat16)
    inc_rows = incoming.reshape(ghost_total, brick_rows, channels)
    inputs = (
        jnp.einsum("pb,bvd->pvd", in_pick[:, :brick_total], own_rows, preferred_element_type=jnp.float32)
        + jnp.einsum("pb,bvd->pvd", in_pick[:, brick_total:], inc_rows, preferred_element_type=jnp.float32)
    ).astype(jnp.bfloat16)
    inputs = inputs.reshape(tap_total, slot_total, brick_rows, channels)
    contrib = jnp.einsum("tsvc,tcd->tsvd", inputs, weights, preferred_element_type=jnp.float32)
    out_pick = _onehot(tgt, brick_total, jnp.float32).T
    produced = jnp.einsum(
        "ip,pvd->ivd", out_pick, contrib.reshape(pair_total, brick_rows, channels),
        precision=lax.Precision.HIGHEST, preferred_element_type=jnp.float32,
    ).astype(jnp.bfloat16)

    partial_value = jnp.einsum(
        "tsvc,tsvd->tcd", inputs, upstream, preferred_element_type=jnp.float32
    )
    divisor = jnp.float32(4 * lax.axis_size("dp") * lax.axis_size("fsdp"))
    scattered = lax.psum_scatter(partial_value, "fsdp", scatter_dimension=1, tiled=True)
    kernel_grad = _halving_doubling_sum(scattered, "dp") / divisor

    owner_pick = _onehot(senders.reshape(-1), brick_total, jnp.bfloat16).T
    back_sum = jnp.einsum(
        "ip,pvd->ivd", owner_pick, returned.reshape(ghost_total, brick_rows, channels),
        preferred_element_type=jnp.float32,
    )
    in_grad = (own_grad + back_sum).astype(jnp.bfloat16)
    return (produced[None, None], in_grad[None, None], kernel_grad)


def solution(mesh):
    placed = (
        P("dp", "fsdp", None, None, None),
        P("dp", "fsdp", None, None, None),
        P(None, "fsdp", None),
        P("dp", "fsdp", None, None),
        P("dp", "fsdp", None, None, None),
        P("dp", "fsdp", None),
    )
    return jax.shard_map(
        on_device,
        mesh=mesh,
        in_specs=placed,
        out_specs=(
            P("dp", "fsdp", None, None, None),
            P("dp", "fsdp", None, None, None),
            P(None, "fsdp", None),
        ),
        check_vma=False,
    )
```

```python
import jax
import jax.numpy as jnp
from jax import lax
from jax.sharding import PartitionSpec as P


def _onehot(index, size, dtype):
    return (index[..., None] == jnp.arange(size, dtype=index.dtype)).astype(dtype)


def _halving_doubling_sum(value, axis):
    size = lax.axis_size(axis)
    steps = size.bit_length() - 1
    assert 1 << steps == size
    me = lax.axis_index(axis)
    shape = value.shape
    buf = value.reshape(-1)
    total = buf.shape[0]
    assert total % size == 0
    for k in range(steps):
        half = buf.shape[0] // 2
        bit = (me >> k) & 1
        keep = lax.dynamic_slice_in_dim(buf, bit * half, half)
        send = lax.dynamic_slice_in_dim(buf, (1 - bit) * half, half)
        pairs = [(i, i ^ (1 << k)) for i in range(size)]
        buf = keep + lax.ppermute(send, axis, pairs)
    for k in reversed(range(steps)):
        part = buf.shape[0]
        bit = (me >> k) & 1
        pairs = [(i, i ^ (1 << k)) for i in range(size)]
        other = lax.ppermute(buf, axis, pairs)
        whole = jnp.zeros((2 * part,), buf.dtype)
        whole = lax.dynamic_update_slice_in_dim(whole, buf, bit * part, 0)
        buf = lax.dynamic_update_slice_in_dim(whole, other, (1 - bit) * part, 0)
    return buf.reshape(shape)


def on_device(feats, grad_out, kernel, send_bricks, kmap, pair_count):
    own_rows = feats[0, 0]
    upstream_rows = grad_out[0, 0]
    senders = send_bricks[0, 0]
    peer_total, slot_cap = senders.shape
    brick_total, brick_rows, channels = own_rows.shape
    ghost_total = peer_total * slot_cap
    own_flat = own_rows.reshape(brick_total, brick_rows * channels)
    up_flat = upstream_rows.reshape(brick_total, brick_rows * channels)

    send_pick = _onehot(senders.reshape(-1), brick_total, jnp.bfloat16)
    outgoing = jnp.dot(send_pick, own_flat, preferred_element_type=jnp.float32).astype(jnp.bfloat16)
    outgoing = outgoing.reshape(peer_total, slot_cap, brick_rows, channels)
    incoming = lax.all_to_all(outgoing, "dp", split_axis=0, concat_axis=0, tiled=True)

    weights = lax.all_gather(kernel, "fsdp", axis=1, tiled=True)
    source_map = kmap[0, 0, :, 0, :]
    target_map = kmap[0, 0, :, 1, :]
    counts = pair_count[0, 0]
    tap_total, slot_total = source_map.shape
    pair_total = tap_total * slot_total
    active = jnp.arange(slot_total)[None, :] < counts[:, None]
    src = source_map.reshape(-1)
    tgt = target_map.reshape(-1)
    live = active.reshape(-1)

    up_pick = _onehot(tgt, brick_total, jnp.bfloat16) * live[:, None].astype(jnp.bfloat16)
    upstream = jnp.dot(up_pick, up_flat, preferred_element_type=jnp.float32).astype(jnp.bfloat16)
    upstream = upstream.reshape(tap_total, slot_total, brick_rows, channels)
    backward = jnp.einsum("tsvd,tcd->tsvc", upstream, weights, preferred_element_type=jnp.float32)
    backward = backward.reshape(pair_total, brick_rows * channels)
    src_pick = _onehot(src, brick_total + ghost_total, jnp.float32).T
    ghost_grad = jnp.dot(
        src_pick[brick_total:], backward, precision=lax.Precision.HIGHEST,
        preferred_element_type=jnp.float32,
    ).astype(jnp.bfloat16)
    own_grad = jnp.dot(
        src_pick[:brick_total], backward, precision=lax.Precision.HIGHEST,
        preferred_element_type=jnp.float32,
    )
    incoming, ghost_grad = lax.optimization_barrier((incoming, ghost_grad))
    returned = lax.all_to_all(
        ghost_grad.reshape(peer_total, slot_cap, brick_rows, channels),
        "dp", split_axis=0, concat_axis=0, tiled=True,
    )

    in_pick = _onehot(src, brick_total + ghost_total, jnp.bfloat16) * live[:, None].astype(jnp.bfloat16)
    inc_flat = incoming.reshape(ghost_total, brick_rows * channels)
    inputs = (
        jnp.dot(in_pick[:, :brick_total], own_flat, preferred_element_type=jnp.float32)
        + jnp.dot(in_pick[:, brick_total:], inc_flat, preferred_element_type=jnp.float32)
    ).astype(jnp.bfloat16)
    inputs = inputs.reshape(tap_total, slot_total, brick_rows, channels)
    contrib = jnp.einsum("tsvc,tcd->tsvd", inputs, weights, preferred_element_type=jnp.float32)
    out_pick = _onehot(tgt, brick_total, jnp.float32).T
    produced = jnp.dot(
        out_pick, contrib.reshape(pair_total, brick_rows * channels),
        precision=lax.Precision.HIGHEST, preferred_element_type=jnp.float32,
    )
    produced = produced.reshape(brick_total, brick_rows, channels).astype(jnp.bfloat16)

    partial_value = jnp.einsum(
        "tsvc,tsvd->tcd", inputs, upstream, preferred_element_type=jnp.float32
    )
    divisor = jnp.float32(4 * lax.axis_size("dp") * lax.axis_size("fsdp"))
    scattered = lax.psum_scatter(partial_value, "fsdp", scatter_dimension=1, tiled=True)
    scattered, returned = lax.optimization_barrier((scattered, returned))
    kernel_grad = _halving_doubling_sum(scattered, "dp") / divisor

    owner_pick = _onehot(senders.reshape(-1), brick_total, jnp.bfloat16).T
    back_sum = jnp.dot(
        owner_pick, returned.reshape(ghost_total, brick_rows * channels),
        preferred_element_type=jnp.float32,
    )
    in_grad = (own_grad + back_sum).reshape(brick_total, brick_rows, channels).astype(jnp.bfloat16)
    return (produced[None, None], in_grad[None, None], kernel_grad)


def solution(mesh):
    placed = (
        P("dp", "fsdp", None, None, None),
        P("dp", "fsdp", None, None, None),
        P(None, "fsdp", None),
        P("dp", "fsdp", None, None),
        P("dp", "fsdp", None, None, None),
        P("dp", "fsdp", None),
    )
    return jax.shard_map(
        on_device,
        mesh=mesh,
        in_specs=placed,
        out_specs=(
            P("dp", "fsdp", None, None, None),
            P("dp", "fsdp", None, None, None),
            P(None, "fsdp", None),
        ),
        check_vma=False,
    )
```

```python
import jax
import jax.numpy as jnp
from jax import lax
from jax.sharding import PartitionSpec as P


def _onehot(index, size, dtype):
    return (index[..., None] == jnp.arange(size, dtype=index.dtype)).astype(dtype)


def _halve(buf, axis, k):
    size = lax.axis_size(axis)
    me = lax.axis_index(axis)
    half = buf.shape[0] // 2
    bit = (me >> k) & 1
    keep = lax.dynamic_slice_in_dim(buf, bit * half, half)
    send = lax.dynamic_slice_in_dim(buf, (1 - bit) * half, half)
    pairs = [(i, i ^ (1 << k)) for i in range(size)]
    return keep + lax.ppermute(send, axis, pairs)


def _double(buf, axis, k):
    size = lax.axis_size(axis)
    me = lax.axis_index(axis)
    part = buf.shape[0]
    bit = (me >> k) & 1
    pairs = [(i, i ^ (1 << k)) for i in range(size)]
    other = lax.ppermute(buf, axis, pairs)
    whole = jnp.zeros((2 * part,), buf.dtype)
    whole = lax.dynamic_update_slice_in_dim(whole, buf, bit * part, 0)
    return lax.dynamic_update_slice_in_dim(whole, other, (1 - bit) * part, 0)


def on_device(feats, grad_out, kernel, send_bricks, kmap, pair_count):
    own_rows = feats[0, 0]
    upstream_rows = grad_out[0, 0]
    senders = send_bricks[0, 0]
    peer_total, slot_cap = senders.shape
    brick_total, brick_rows, channels = own_rows.shape
    ghost_total = peer_total * slot_cap
    own_flat = own_rows.reshape(brick_total, brick_rows * channels)
    up_flat = upstream_rows.reshape(brick_total, brick_rows * channels)

    send_pick = _onehot(senders.reshape(-1), brick_total, jnp.bfloat16)
    outgoing = jnp.dot(send_pick, own_flat, preferred_element_type=jnp.float32).astype(jnp.bfloat16)
    outgoing = outgoing.reshape(peer_total, slot_cap, brick_rows, channels)
    incoming = lax.all_to_all(outgoing, "dp", split_axis=0, concat_axis=0, tiled=True)

    weights = lax.all_gather(kernel, "fsdp", axis=1, tiled=True)
    source_map = kmap[0, 0, :, 0, :]
    target_map = kmap[0, 0, :, 1, :]
    counts = pair_count[0, 0]
    tap_total, slot_total = source_map.shape
    pair_total = tap_total * slot_total
    active = jnp.arange(slot_total)[None, :] < counts[:, None]
    src = source_map.reshape(-1)
    tgt = target_map.reshape(-1)
    live = active.reshape(-1)

    up_pick = _onehot(tgt, brick_total, jnp.bfloat16) * live[:, None].astype(jnp.bfloat16)
    upstream = jnp.dot(up_pick, up_flat, preferred_element_type=jnp.float32).astype(jnp.bfloat16)
    upstream = upstream.reshape(tap_total, slot_total, brick_rows, channels)
    backward = jnp.einsum("tsvd,tcd->tsvc", upstream, weights, preferred_element_type=jnp.float32)
    backward = backward.reshape(pair_total, brick_rows * channels)
    src_pick = _onehot(src, brick_total + ghost_total, jnp.float32).T
    ghost_grad = jnp.dot(
        src_pick[brick_total:], backward, precision=lax.Precision.HIGHEST,
        preferred_element_type=jnp.float32,
    ).astype(jnp.bfloat16)
    own_grad = jnp.dot(
        src_pick[:brick_total], backward, precision=lax.Precision.HIGHEST,
        preferred_element_type=jnp.float32,
    )
    incoming, ghost_grad = lax.optimization_barrier((incoming, ghost_grad))
    returned = lax.all_to_all(
        ghost_grad.reshape(peer_total, slot_cap, brick_rows, channels),
        "dp", split_axis=0, concat_axis=0, tiled=True,
    )

    in_pick = _onehot(src, brick_total + ghost_total, jnp.bfloat16) * live[:, None].astype(jnp.bfloat16)
    inc_flat = incoming.reshape(ghost_total, brick_rows * channels)
    inputs = (
        jnp.dot(in_pick[:, :brick_total], own_flat, preferred_element_type=jnp.float32)
        + jnp.dot(in_pick[:, brick_total:], inc_flat, preferred_element_type=jnp.float32)
    ).astype(jnp.bfloat16)
    inputs = inputs.reshape(tap_total, slot_total, brick_rows, channels)
    contrib = jnp.einsum("tsvc,tcd->tsvd", inputs, weights, preferred_element_type=jnp.float32)
    out_pick = _onehot(tgt, brick_total, jnp.float32).T
    produced = jnp.dot(
        out_pick, contrib.reshape(pair_total, brick_rows * channels),
        precision=lax.Precision.HIGHEST, preferred_element_type=jnp.float32,
    )
    produced = produced.reshape(brick_total, brick_rows, channels).astype(jnp.bfloat16)

    partial_value = jnp.einsum(
        "tsvc,tsvd->tcd", inputs, upstream, preferred_element_type=jnp.float32
    )
    divisor = jnp.float32(4 * lax.axis_size("dp") * lax.axis_size("fsdp"))
    scattered = lax.psum_scatter(partial_value, "fsdp", scatter_dimension=1, tiled=True)
    steps = lax.axis_size("dp").bit_length() - 1
    assert 1 << steps == lax.axis_size("dp")
    early = min(3, steps)
    buf = scattered.reshape(-1)
    assert buf.shape[0] % lax.axis_size("dp") == 0
    for k in range(early):
        buf = _halve(buf, "dp", k)
    buf, returned, produced, own_grad = lax.optimization_barrier((buf, returned, produced, own_grad))
    for k in range(early, steps):
        buf = _halve(buf, "dp", k)
    for k in reversed(range(steps)):
        buf = _double(buf, "dp", k)
    kernel_grad = buf.reshape(scattered.shape) / divisor

    owner_pick = _onehot(senders.reshape(-1), brick_total, jnp.bfloat16).T
    back_sum = jnp.dot(
        owner_pick, returned.reshape(ghost_total, brick_rows * channels),
        preferred_element_type=jnp.float32,
    )
    in_grad = (own_grad + back_sum).reshape(brick_total, brick_rows, channels).astype(jnp.bfloat16)
    return (produced[None, None], in_grad[None, None], kernel_grad)


def solution(mesh):
    placed = (
        P("dp", "fsdp", None, None, None),
        P("dp", "fsdp", None, None, None),
        P(None, "fsdp", None),
        P("dp", "fsdp", None, None),
        P("dp", "fsdp", None, None, None),
        P("dp", "fsdp", None),
    )
    return jax.shard_map(
        on_device,
        mesh=mesh,
        in_specs=placed,
        out_specs=(
            P("dp", "fsdp", None, None, None),
            P("dp", "fsdp", None, None, None),
            P(None, "fsdp", None),
        ),
        check_vma=False,
    )
```

```python
import jax
import jax.numpy as jnp
from jax import lax
from jax.sharding import PartitionSpec as P


def _onehot(index, size, dtype):
    return (index[..., None] == jnp.arange(size, dtype=index.dtype)).astype(dtype)


def _halve(buf, axis, k):
    size = lax.axis_size(axis)
    me = lax.axis_index(axis)
    half = buf.shape[0] // 2
    bit = (me >> k) & 1
    keep = lax.dynamic_slice_in_dim(buf, bit * half, half)
    send = lax.dynamic_slice_in_dim(buf, (1 - bit) * half, half)
    pairs = [(i, i ^ (1 << k)) for i in range(size)]
    return keep + lax.ppermute(send, axis, pairs)


def _double(buf, axis, k):
    size = lax.axis_size(axis)
    me = lax.axis_index(axis)
    bit = (me >> k) & 1
    pairs = [(i, i ^ (1 << k)) for i in range(size)]
    other = lax.ppermute(buf, axis, pairs)
    low_first = jnp.concatenate([buf, other])
    high_first = jnp.concatenate([other, buf])
    return jnp.where(bit == 0, low_first, high_first)


def _section(feats, grad_out, kernel, send_bricks, kmap, pair_count):
    own_rows = feats[0, 0]
    upstream_rows = grad_out[0, 0]
    senders = send_bricks[0, 0]
    peer_total, slot_cap = senders.shape
    brick_total, brick_rows, channels = own_rows.shape
    ghost_total = peer_total * slot_cap
    own_flat = own_rows.reshape(brick_total, brick_rows * channels)
    up_flat = upstream_rows.reshape(brick_total, brick_rows * channels)

    send_pick = _onehot(senders.reshape(-1), brick_total, jnp.bfloat16)
    outgoing = jnp.dot(send_pick, own_flat, preferred_element_type=jnp.float32).astype(jnp.bfloat16)
    outgoing = outgoing.reshape(peer_total, slot_cap, brick_rows, channels)
    incoming = lax.all_to_all(outgoing, "dp", split_axis=0, concat_axis=0, tiled=True)

    weights = lax.all_gather(kernel, "fsdp", axis=1, tiled=True)
    source_map = kmap[0, 0, :, 0, :]
    target_map = kmap[0, 0, :, 1, :]
    counts = pair_count[0, 0]
    tap_total, slot_total = source_map.shape
    pair_total = tap_total * slot_total
    active = jnp.arange(slot_total)[None, :] < counts[:, None]
    src = source_map.reshape(-1)
    tgt = target_map.reshape(-1)
    live = active.reshape(-1)

    up_pick = _onehot(tgt, brick_total, jnp.bfloat16) * live[:, None].astype(jnp.bfloat16)
    upstream = jnp.dot(up_pick, up_flat, preferred_element_type=jnp.float32).astype(jnp.bfloat16)
    upstream = upstream.reshape(tap_total, slot_total, brick_rows, channels)
    backward = jnp.einsum("tsvd,tcd->tsvc", upstream, weights, preferred_element_type=jnp.float32)
    backward = backward.reshape(pair_total, brick_rows * channels)
    src_pick = _onehot(src, brick_total + ghost_total, jnp.float32).T
    ghost_grad = jnp.dot(
        src_pick[brick_total:], backward, precision=lax.Precision.HIGHEST,
        preferred_element_type=jnp.float32,
    ).astype(jnp.bfloat16)
    own_grad = jnp.dot(
        src_pick[:brick_total], backward, precision=lax.Precision.HIGHEST,
        preferred_element_type=jnp.float32,
    )
    returned = lax.all_to_all(
        ghost_grad.reshape(peer_total, slot_cap, brick_rows, channels),
        "dp", split_axis=0, concat_axis=0, tiled=True,
    )

    in_pick = _onehot(src, brick_total + ghost_total, jnp.bfloat16) * live[:, None].astype(jnp.bfloat16)
    inc_flat = incoming.reshape(ghost_total, brick_rows * channels)
    inputs = (
        jnp.dot(in_pick[:, :brick_total], own_flat, preferred_element_type=jnp.float32)
        + jnp.dot(in_pick[:, brick_total:], inc_flat, preferred_element_type=jnp.float32)
    ).astype(jnp.bfloat16)
    inputs = inputs.reshape(tap_total, slot_total, brick_rows, channels)
    contrib = jnp.einsum("tsvc,tcd->tsvd", inputs, weights, preferred_element_type=jnp.float32)
    out_pick = _onehot(tgt, brick_total, jnp.float32).T
    produced = jnp.dot(
        out_pick, contrib.reshape(pair_total, brick_rows * channels),
        precision=lax.Precision.HIGHEST, preferred_element_type=jnp.float32,
    )
    produced = produced.reshape(brick_total, brick_rows, channels).astype(jnp.bfloat16)

    partial_value = jnp.einsum(
        "tsvc,tsvd->tcd", inputs, upstream, preferred_element_type=jnp.float32
    )
    divisor = jnp.float32(4 * lax.axis_size("dp") * lax.axis_size("fsdp"))
    scattered = lax.psum_scatter(partial_value, "fsdp", scatter_dimension=1, tiled=True)
    steps = lax.axis_size("dp").bit_length() - 1
    assert 1 << steps == lax.axis_size("dp")
    early = min(3, steps)
    buf = scattered.reshape(-1)
    assert buf.shape[0] % lax.axis_size("dp") == 0
    for k in range(early):
        buf = _halve(buf, "dp", k)
    buf, returned, produced, own_grad = lax.optimization_barrier((buf, returned, produced, own_grad))
    for k in range(early, steps):
        buf = _halve(buf, "dp", k)
    for k in reversed(range(steps)):
        buf = _double(buf, "dp", k)
    kernel_grad = buf.reshape(scattered.shape) / divisor

    owner_pick = _onehot(senders.reshape(-1), brick_total, jnp.bfloat16).T
    back_sum = jnp.dot(
        owner_pick, returned.reshape(ghost_total, brick_rows * channels),
        preferred_element_type=jnp.float32,
    )
    in_grad = (own_grad + back_sum).reshape(brick_total, brick_rows, channels).astype(jnp.bfloat16)
    return (produced[None, None], in_grad[None, None], kernel_grad)


def solution(mesh):
    placed = (
        P("dp", "fsdp", None, None, None),
        P("dp", "fsdp", None, None, None),
        P(None, "fsdp", None),
        P("dp", "fsdp", None, None),
        P("dp", "fsdp", None, None, None),
        P("dp", "fsdp", None),
    )
    return jax.shard_map(
        _section,
        mesh=mesh,
        in_specs=placed,
        out_specs=(
            P("dp", "fsdp", None, None, None),
            P("dp", "fsdp", None, None, None),
            P(None, "fsdp", None),
        ),
        check_vma=False,
    )
```

```python
import jax
import jax.numpy as jnp
from jax import lax
from jax.sharding import PartitionSpec as P


def _onehot(index, size, dtype):
    return (index[..., None] == jnp.arange(size, dtype=index.dtype)).astype(dtype)


def _direct_sum(buf, axis, low, width):
    size = lax.axis_size(axis)
    group = 1 << width
    me = lax.axis_index(axis)
    mine = (me >> low) & (group - 1)
    part = buf.shape[0] // group
    chunks = buf.reshape(group, part)
    total = lax.dynamic_index_in_dim(chunks, mine, 0, keepdims=False)
    for j in range(1, group):
        pairs = [(i, i ^ (j << low)) for i in range(size)]
        send = lax.dynamic_index_in_dim(chunks, mine ^ j, 0, keepdims=False)
        total = total + lax.ppermute(send, axis, pairs)
    gathered = [total]
    for j in range(1, group):
        pairs = [(i, i ^ (j << low)) for i in range(size)]
        gathered.append(lax.ppermute(total, axis, pairs))
    stacked = jnp.stack(gathered)
    order = jnp.arange(group, dtype=mine.dtype) ^ mine
    return jnp.take(stacked, order, axis=0).reshape(-1)


def _halve(buf, axis, k):
    size = lax.axis_size(axis)
    me = lax.axis_index(axis)
    half = buf.shape[0] // 2
    bit = (me >> k) & 1
    keep = lax.dynamic_slice_in_dim(buf, bit * half, half)
    send = lax.dynamic_slice_in_dim(buf, (1 - bit) * half, half)
    pairs = [(i, i ^ (1 << k)) for i in range(size)]
    return keep + lax.ppermute(send, axis, pairs)


def _double(buf, axis, k):
    size = lax.axis_size(axis)
    me = lax.axis_index(axis)
    bit = (me >> k) & 1
    pairs = [(i, i ^ (1 << k)) for i in range(size)]
    other = lax.ppermute(buf, axis, pairs)
    low_first = jnp.concatenate([buf, other])
    high_first = jnp.concatenate([other, buf])
    return jnp.where(bit == 0, low_first, high_first)


def _section(feats, grad_out, kernel, send_bricks, kmap, pair_count):
    own_rows = feats[0, 0]
    upstream_rows = grad_out[0, 0]
    senders = send_bricks[0, 0]
    peer_total, slot_cap = senders.shape
    brick_total, brick_rows, channels = own_rows.shape
    ghost_total = peer_total * slot_cap
    own_flat = own_rows.reshape(brick_total, brick_rows * channels)
    up_flat = upstream_rows.reshape(brick_total, brick_rows * channels)

    send_pick = _onehot(senders.reshape(-1), brick_total, jnp.bfloat16)
    outgoing = jnp.dot(send_pick, own_flat, preferred_element_type=jnp.float32).astype(jnp.bfloat16)
    outgoing = outgoing.reshape(peer_total, slot_cap, brick_rows, channels)
    incoming = lax.all_to_all(outgoing, "dp", split_axis=0, concat_axis=0, tiled=True)

    weights = lax.all_gather(kernel, "fsdp", axis=1, tiled=True)
    source_map = kmap[0, 0, :, 0, :]
    target_map = kmap[0, 0, :, 1, :]
    counts = pair_count[0, 0]
    tap_total, slot_total = source_map.shape
    pair_total = tap_total * slot_total
    active = jnp.arange(slot_total)[None, :] < counts[:, None]
    src = source_map.reshape(-1)
    tgt = target_map.reshape(-1)
    live = active.reshape(-1)

    up_pick = _onehot(tgt, brick_total, jnp.bfloat16) * live[:, None].astype(jnp.bfloat16)
    upstream = jnp.dot(up_pick, up_flat, preferred_element_type=jnp.float32).astype(jnp.bfloat16)
    upstream = upstream.reshape(tap_total, slot_total, brick_rows, channels)
    backward = jnp.einsum("tsvd,tcd->tsvc", upstream, weights, preferred_element_type=jnp.float32)
    backward = backward.reshape(pair_total, brick_rows * channels)
    src_pick = _onehot(src, brick_total + ghost_total, jnp.float32).T
    ghost_grad = jnp.dot(
        src_pick[brick_total:], backward, precision=lax.Precision.HIGHEST,
        preferred_element_type=jnp.float32,
    ).astype(jnp.bfloat16)
    own_grad = jnp.dot(
        src_pick[:brick_total], backward, precision=lax.Precision.HIGHEST,
        preferred_element_type=jnp.float32,
    )
    returned = lax.all_to_all(
        ghost_grad.reshape(peer_total, slot_cap, brick_rows, channels),
        "dp", split_axis=0, concat_axis=0, tiled=True,
    )

    in_pick = _onehot(src, brick_total + ghost_total, jnp.bfloat16) * live[:, None].astype(jnp.bfloat16)
    inc_flat = incoming.reshape(ghost_total, brick_rows * channels)
    inputs = (
        jnp.dot(in_pick[:, :brick_total], own_flat, preferred_element_type=jnp.float32)
        + jnp.dot(in_pick[:, brick_total:], inc_flat, preferred_element_type=jnp.float32)
    ).astype(jnp.bfloat16)
    inputs = inputs.reshape(tap_total, slot_total, brick_rows, channels)
    contrib = jnp.einsum("tsvc,tcd->tsvd", inputs, weights, preferred_element_type=jnp.float32)
    out_pick = _onehot(tgt, brick_total, jnp.float32).T
    produced = jnp.dot(
        out_pick, contrib.reshape(pair_total, brick_rows * channels),
        precision=lax.Precision.HIGHEST, preferred_element_type=jnp.float32,
    )
    produced = produced.reshape(brick_total, brick_rows, channels).astype(jnp.bfloat16)

    partial_value = jnp.einsum(
        "tsvc,tsvd->tcd", inputs, upstream, preferred_element_type=jnp.float32
    )
    divisor = jnp.float32(4 * lax.axis_size("dp") * lax.axis_size("fsdp"))
    scattered = lax.psum_scatter(partial_value, "fsdp", scatter_dimension=1, tiled=True)
    steps = lax.axis_size("dp").bit_length() - 1
    assert 1 << steps == lax.axis_size("dp")
    early = min(3, steps)
    buf = scattered.reshape(-1)
    assert buf.shape[0] % lax.axis_size("dp") == 0
    for k in range(early):
        buf = _halve(buf, "dp", k)
    buf, returned, produced, own_grad = lax.optimization_barrier((buf, returned, produced, own_grad))
    if steps > early:
        buf = _direct_sum(buf, "dp", early, steps - early)
    for k in reversed(range(early)):
        buf = _double(buf, "dp", k)
    kernel_grad = buf.reshape(scattered.shape) / divisor

    owner_pick = _onehot(senders.reshape(-1), brick_total, jnp.bfloat16).T
    back_sum = jnp.dot(
        owner_pick, returned.reshape(ghost_total, brick_rows * channels),
        preferred_element_type=jnp.float32,
    )
    in_grad = (own_grad + back_sum).reshape(brick_total, brick_rows, channels).astype(jnp.bfloat16)
    return (produced[None, None], in_grad[None, None], kernel_grad)


def solution(mesh):
    placed = (
        P("dp", "fsdp", None, None, None),
        P("dp", "fsdp", None, None, None),
        P(None, "fsdp", None),
        P("dp", "fsdp", None, None),
        P("dp", "fsdp", None, None, None),
        P("dp", "fsdp", None),
    )
    return jax.shard_map(
        _section,
        mesh=mesh,
        in_specs=placed,
        out_specs=(
            P("dp", "fsdp", None, None, None),
            P("dp", "fsdp", None, None, None),
            P(None, "fsdp", None),
        ),
        check_vma=False,
    )
```

```python
import jax
import jax.numpy as jnp
from jax import lax
from jax.sharding import PartitionSpec as P


def _onehot(index, size, dtype):
    return (index[..., None] == jnp.arange(size, dtype=index.dtype)).astype(dtype)


def _halve(buf, axis, k):
    size = lax.axis_size(axis)
    me = lax.axis_index(axis)
    half = buf.shape[0] // 2
    bit = (me >> k) & 1
    keep = lax.dynamic_slice_in_dim(buf, bit * half, half)
    send = lax.dynamic_slice_in_dim(buf, (1 - bit) * half, half)
    pairs = [(i, i ^ (1 << k)) for i in range(size)]
    return keep + lax.ppermute(send, axis, pairs)


def _double(buf, axis, k):
    size = lax.axis_size(axis)
    me = lax.axis_index(axis)
    bit = (me >> k) & 1
    pairs = [(i, i ^ (1 << k)) for i in range(size)]
    other = lax.ppermute(buf, axis, pairs)
    low_first = jnp.concatenate([buf, other])
    high_first = jnp.concatenate([other, buf])
    return jnp.where(bit == 0, low_first, high_first)


def _section(feats, grad_out, kernel, send_bricks, kmap, pair_count):
    own_rows = feats[0, 0]
    upstream_rows = grad_out[0, 0]
    senders = send_bricks[0, 0]
    peer_total, slot_cap = senders.shape
    brick_total, brick_rows, channels = own_rows.shape
    ghost_total = peer_total * slot_cap
    own_flat = own_rows.reshape(brick_total, brick_rows * channels)
    up_flat = upstream_rows.reshape(brick_total, brick_rows * channels)

    filled = senders >= 0
    outgoing = jnp.where(
        filled[:, :, None, None], own_rows[jnp.maximum(senders, 0)], jnp.zeros((), own_rows.dtype)
    )
    incoming = lax.all_to_all(outgoing, "dp", split_axis=0, concat_axis=0, tiled=True)

    weights = lax.all_gather(kernel, "fsdp", axis=1, tiled=True)
    source_map = kmap[0, 0, :, 0, :]
    target_map = kmap[0, 0, :, 1, :]
    counts = pair_count[0, 0]
    tap_total, slot_total = source_map.shape
    pair_total = tap_total * slot_total
    active = jnp.arange(slot_total)[None, :] < counts[:, None]
    src = source_map.reshape(-1)
    tgt = target_map.reshape(-1)
    live = active.reshape(-1)

    up_pick = _onehot(tgt, brick_total, jnp.bfloat16) * live[:, None].astype(jnp.bfloat16)
    upstream = jnp.dot(up_pick, up_flat, preferred_element_type=jnp.float32).astype(jnp.bfloat16)
    upstream = upstream.reshape(tap_total, slot_total, brick_rows, channels)
    backward = jnp.einsum("tsvd,tcd->tsvc", upstream, weights, preferred_element_type=jnp.float32)
    backward = backward.reshape(pair_total, brick_rows * channels)
    src_pick = _onehot(src, brick_total + ghost_total, jnp.float32).T
    ghost_grad = jnp.dot(
        src_pick[brick_total:], backward, precision=lax.Precision.HIGHEST,
        preferred_element_type=jnp.float32,
    ).astype(jnp.bfloat16)
    own_grad = jnp.dot(
        src_pick[:brick_total], backward, precision=lax.Precision.HIGHEST,
        preferred_element_type=jnp.float32,
    )
    returned = lax.all_to_all(
        ghost_grad.reshape(peer_total, slot_cap, brick_rows, channels),
        "dp", split_axis=0, concat_axis=0, tiled=True,
    )

    in_pick = _onehot(src, brick_total + ghost_total, jnp.bfloat16) * live[:, None].astype(jnp.bfloat16)
    inc_flat = incoming.reshape(ghost_total, brick_rows * channels)
    inputs = (
        jnp.dot(in_pick[:, :brick_total], own_flat, preferred_element_type=jnp.float32)
        + jnp.dot(in_pick[:, brick_total:], inc_flat, preferred_element_type=jnp.float32)
    ).astype(jnp.bfloat16)
    inputs = inputs.reshape(tap_total, slot_total, brick_rows, channels)
    contrib = jnp.einsum("tsvc,tcd->tsvd", inputs, weights, preferred_element_type=jnp.float32)
    out_pick = _onehot(tgt, brick_total, jnp.float32).T
    produced = jnp.dot(
        out_pick, contrib.reshape(pair_total, brick_rows * channels),
        precision=lax.Precision.HIGHEST, preferred_element_type=jnp.float32,
    )
    produced = produced.reshape(brick_total, brick_rows, channels).astype(jnp.bfloat16)

    partial_value = jnp.einsum(
        "tsvc,tsvd->tcd", inputs, upstream, preferred_element_type=jnp.float32
    )
    divisor = jnp.float32(4 * lax.axis_size("dp") * lax.axis_size("fsdp"))
    scattered = lax.psum_scatter(partial_value, "fsdp", scatter_dimension=1, tiled=True)
    steps = lax.axis_size("dp").bit_length() - 1
    assert 1 << steps == lax.axis_size("dp")
    early = min(3, steps)
    buf = scattered.reshape(-1)
    assert buf.shape[0] % lax.axis_size("dp") == 0
    for k in range(early):
        buf = _halve(buf, "dp", k)
    buf, returned, produced, own_grad = lax.optimization_barrier((buf, returned, produced, own_grad))
    for k in range(early, steps):
        buf = _halve(buf, "dp", k)
    buf = buf / divisor
    for k in reversed(range(steps)):
        buf = _double(buf, "dp", k)
    kernel_grad = buf.reshape(scattered.shape)

    owner_pick = _onehot(senders.reshape(-1), brick_total, jnp.bfloat16).T
    back_sum = jnp.dot(
        owner_pick, returned.reshape(ghost_total, brick_rows * channels),
        preferred_element_type=jnp.float32,
    )
    in_grad = (own_grad + back_sum).reshape(brick_total, brick_rows, channels).astype(jnp.bfloat16)
    return (produced[None, None], in_grad[None, None], kernel_grad)


def solution(mesh):
    placed = (
        P("dp", "fsdp", None, None, None),
        P("dp", "fsdp", None, None, None),
        P(None, "fsdp", None),
        P("dp", "fsdp", None, None),
        P("dp", "fsdp", None, None, None),
        P("dp", "fsdp", None),
    )
    return jax.shard_map(
        _section,
        mesh=mesh,
        in_specs=placed,
        out_specs=(
            P("dp", "fsdp", None, None, None),
            P("dp", "fsdp", None, None, None),
            P(None, "fsdp", None),
        ),
        check_vma=False,
    )
```
